512 devices in a mesh: ctx: 64 (over x_hi, z, core), mp: 8 (over x_lo, y).
Axes of the slice: x: 4 (x_hi: 2, x_lo: 2; x = x_hi * 2 + x_lo), y: 4, z: 16, core: 2. Of those that a mesh axis runs over, the one named last changes fastest.
Arguments:
- queries: bfloat16 [4096, 8192], P('ctx', 'mp'), may hold values from -8 to 8
- keys: bfloat16 [4096, 1024], P('ctx', 'mp'), may hold values from -8 to 8
- values: bfloat16 [4096, 1024], P('ctx', 'mp'), may hold values from -6 to 6
- positions: int32 [4096], P('ctx'), may hold values from 0 to 4095, as said below
- x_normed: bfloat16 [4096, 8192], P('ctx', 'mp'), may hold values from -6 to 6
- w_gate: bfloat16 [8192, 16384], P('mp', 'ctx'), may hold values from -0.0625 to 0.0625
- w_up: bfloat16 [8192, 16384], P('mp', 'ctx'), may hold values from -0.0625 to 0.0625
Outputs:
- attended: bfloat16 [4096, 8192], P('ctx', 'mp')
- mlp_hidden: bfloat16 [4096, 16384], P('mp', 'ctx')
The draws below stay inside these ranges and needn't reach their ends.
Inputs may be any that keep to these rules, and one draw needn't show every extreme that they name: `positions`: each position of 0 to 4095 appears exactly once.
All inputs are finite; a program needn't handle non-finite values.
Results may differ from the reference program's by a relative error of at most 0.02.
Values may be sent and summed in bfloat16 or wider, within the bound.
No kernel may reach another device: no remote copies, remote signals or barrier semaphores. Data moves between devices by JAX's collectives and lax.ppermute only.
A program may use at most 64 MiB of HBM per device.

```python
import jax
import jax.numpy as jnp
from jax import lax

HEAD = 128
HEADS = 64
KV_HEADS = 8
FFW = 16384
D = 8192
TOKENS = 4096
GROUP_FEAT = 1024


def make_positions(key):
    return jax.random.permutation(jax.random.fold_in(key, 11), TOKENS).astype(jnp.int32)


def draw_positions(key, part):
    return make_positions(key)


def drawn_pair(key):
    q_key = jax.random.fold_in(key, 21)
    k_key = jax.random.fold_in(key, 22)
    query_base = jnp.clip(jax.random.normal(q_key, (TOKENS, HEADS, HEAD), jnp.float32), -8.0, 8.0)
    key_base = jnp.clip(jax.random.normal(k_key, (TOKENS, KV_HEADS, HEAD), jnp.float32), -8.0, 8.0)
    return (query_base.reshape(TOKENS, HEADS * HEAD), key_base.reshape(TOKENS, KV_HEADS * HEAD))


def draw_queries(key, part):
    return drawn_pair(key)[0].astype(jnp.bfloat16)


def draw_keys(key, part):
    return drawn_pair(key)[1].astype(jnp.bfloat16)


def steps_of(stream_key, extent, cuts, smallest, top_value):
    factor_of = 1.0
    for dim, shards_of in cuts:
        heights = jax.random.uniform(jax.random.fold_in(jax.random.fold_in(stream_key, 6), dim), (shards_of,), jnp.float32, smallest / len(cuts), top_value / len(cuts))
        factor_of = factor_of * jnp.repeat(jnp.exp(heights), extent[dim] // shards_of).reshape((-1,) + (1,) * (len(extent) - 1 - dim))
    return factor_of


def centred(stream_key, dims, deviation, reach, shards=(), kind=jnp.bfloat16):
    entries = jax.random.normal(stream_key, dims, jnp.float32) * deviation
    if len(shards) > 0:
        entries = steps_of(stream_key, dims, shards, -0.22, 0.18) * entries
    return jnp.clip(entries, min=-reach, max=reach).astype(kind)


def setup_inputs(seed: int = 0) -> dict:
    seeds = jax.random.split(jax.random.key(seed), 8)
    queries = draw_queries(jax.random.fold_in(seeds[7], 71), 0)
    keys = draw_keys(jax.random.fold_in(seeds[7], 71), 0)
    values = centred(seeds[2], (TOKENS, KV_HEADS * HEAD), 1.0, 6.0, ((0, 64), (1, 8)))
    positions = draw_positions(jax.random.fold_in(seeds[7], 71), 0)
    x_normed = centred(seeds[4], (TOKENS, D), 1.0, 6.0, ((0, 64), (1, 8)))
    w_gate = centred(seeds[5], (D, FFW), D ** -0.5, 0.0625, ((0, 8), (1, 64)))
    w_up = centred(seeds[6], (D, FFW), D ** -0.5, 0.0625, ((0, 8), (1, 64)))
    return {"queries": queries, "keys": keys, "values": values, "positions": positions, "x_normed": x_normed, "w_gate": w_gate, "w_up": w_up}


def reference(queries, keys, values, positions, x_normed, w_gate, w_up):
    group = HEADS // KV_HEADS
    scale = HEAD ** -0.5
    visible = positions[None, :] <= positions[:, None]

    def one_head(head):
        kv_head = head // group
        q_rows = lax.dynamic_slice_in_dim(queries, (head * HEAD).astype(jnp.int32), HEAD, 1)
        k_rows = lax.dynamic_slice_in_dim(keys, (kv_head * HEAD).astype(jnp.int32), HEAD, 1)
        v_rows = lax.dynamic_slice_in_dim(values, (kv_head * HEAD).astype(jnp.int32), HEAD, 1)
        scores = jnp.dot(q_rows, k_rows.T, preferred_element_type=jnp.float32) * scale
        top = jnp.max(jnp.where(visible, scores, jnp.float32(-1e30)), axis=1)
        weights = jnp.where(visible, jnp.exp(scores - top[:, None]), jnp.float32(0.0))
        total = jnp.sum(weights, axis=1)
        mixed = jnp.dot(weights.astype(jnp.bfloat16), v_rows, preferred_element_type=jnp.float32)
        return (mixed / total[:, None]).astype(jnp.bfloat16)

    per_head = lax.map(one_head, jnp.arange(HEADS, dtype=jnp.int32))
    attended = jnp.transpose(per_head, (1, 0, 2)).reshape(TOKENS, HEADS * HEAD)

    blocks = D // GROUP_FEAT
    gate = jnp.zeros((TOKENS, FFW), jnp.float32)
    up = jnp.zeros((TOKENS, FFW), jnp.float32)
    for block in range(blocks):
        x_part = x_normed[:, block * GROUP_FEAT:(block + 1) * GROUP_FEAT]
        g_part = jnp.dot(x_part, w_gate[block * GROUP_FEAT:(block + 1) * GROUP_FEAT], preferred_element_type=jnp.float32)
        u_part = jnp.dot(x_part, w_up[block * GROUP_FEAT:(block + 1) * GROUP_FEAT], preferred_element_type=jnp.float32)
        gate = gate + g_part.astype(jnp.bfloat16).astype(jnp.float32)
        up = up + u_part.astype(jnp.bfloat16).astype(jnp.float32)
    mlp_hidden = (jax.nn.silu(gate) * up).astype(jnp.bfloat16)
    return (attended, mlp_hidden)
```

```python
import jax
import jax.numpy as jnp
from jax import lax
from jax.sharding import PartitionSpec as P

HEAD = 128


def per_device(queries, keys, values, positions, x_normed, w_gate, w_up):
    tok_rows = queries.shape[0]
    local_heads = queries.shape[1] // HEAD
    local_kv = keys.shape[1] // HEAD
    group = local_heads // local_kv
    scale = HEAD ** (-0.5)
    query_four = queries.reshape(tok_rows, local_kv, group, HEAD)
    top_run = jnp.full((local_kv, group, tok_rows), -1e30, jnp.float32)
    pos_hi = positions // 64
    pos_lo = positions - pos_hi * 64
    pos_cols = jnp.zeros((tok_rows, HEAD), jnp.bfloat16)
    pos_cols = pos_cols.at[:, 0].set(pos_hi.astype(jnp.bfloat16))
    pos_cols = pos_cols.at[:, 1].set(pos_lo.astype(jnp.bfloat16))
    kv_pack = jnp.concatenate((keys, values, pos_cols), axis=1)
    kv_all = lax.all_gather(kv_pack, "ctx", axis=0, tiled=True)
    kv_width = keys.shape[1]
    k_piece = kv_all[:, :kv_width]
    v_piece = kv_all[:, kv_width : 2 * kv_width]
    pos_back = kv_all[:, 2 * kv_width :].astype(jnp.float32)
    k_pos = pos_back[:, 0] * 64.0 + pos_back[:, 1]
    q_pos = positions.astype(jnp.float32)
    count = k_piece.shape[0]
    k_three = k_piece.reshape(count, local_kv, HEAD)
    v_three = v_piece.reshape(count, local_kv, HEAD)
    scores = (
        jnp.einsum("tgjd,sgd->gjts", query_four, k_three, preferred_element_type=jnp.float32)
        * scale
    )
    visible = k_pos[None, :] <= q_pos[:, None]
    piece_top = jnp.max(jnp.where(visible, scores, jnp.float32(-1e30)), axis=-1)
    top_new = jnp.maximum(top_run, piece_top)
    weights = jnp.where(visible, jnp.exp(scores - top_new[..., None]), jnp.float32(0.0))
    total_new = jnp.sum(weights, axis=-1)
    mixed = jnp.einsum(
        "gjts,sgd->gjtd", weights.astype(jnp.bfloat16), v_three, preferred_element_type=jnp.float32
    )
    final_state = (top_new, total_new, mixed)
    top_run, total_run, accum = final_state
    normed = accum / total_run[..., None]
    attended = (
        jnp.transpose(normed, (2, 0, 1, 3))
        .reshape(tok_rows, local_heads * HEAD)
        .astype(jnp.bfloat16)
    )
    hidden_cols = w_gate.shape[1]
    both_weights = jnp.concatenate((w_gate, w_up), axis=1)
    block_terms = jnp.dot(
        lax.all_gather(x_normed, "ctx", axis=0, tiled=True),
        both_weights,
        preferred_element_type=jnp.float32,
    ).astype(jnp.bfloat16)
    summed = lax.psum_scatter(
        block_terms.astype(jnp.float32).astype(jnp.bfloat16), "mp", scatter_dimension=0, tiled=True
    ).astype(jnp.float32)
    gate = summed[:, :hidden_cols]
    up = summed[:, hidden_cols:]
    mlp_hidden = (jax.nn.silu(gate) * up).astype(jnp.bfloat16)
    return (attended, mlp_hidden)


def solution(mesh):
    return jax.shard_map(
        per_device,
        mesh=mesh,
        in_specs=(
            P("ctx", "mp"),
            P("ctx", "mp"),
            P("ctx", "mp"),
            P("ctx"),
            P("ctx", "mp"),
            P("mp", "ctx"),
            P("mp", "ctx"),
        ),
        out_specs=(P("ctx", "mp"), P("mp", "ctx")),
        check_vma=False,
    )
```

```python
import jax
import jax.numpy as jnp
from jax import lax
from jax.sharding import Mesh, PartitionSpec as P

HEAD = 128
CTX = ("xh", "zz", "cc")


def per_device(queries, keys, values, positions, x_normed, w_gate, w_up):
    tok_rows = queries.shape[0]
    local_heads = queries.shape[1] // HEAD
    local_kv = keys.shape[1] // HEAD
    group = local_heads // local_kv
    scale = HEAD ** (-0.5)
    query_four = queries.reshape(tok_rows, local_kv, group, HEAD)
    top_run = jnp.full((local_kv, group, tok_rows), -1e30, jnp.float32)
    pos_hi = positions // 64
    pos_lo = positions - pos_hi * 64
    pos_cols = jnp.zeros((tok_rows, HEAD), jnp.bfloat16)
    pos_cols = pos_cols.at[:, 0].set(pos_hi.astype(jnp.bfloat16))
    pos_cols = pos_cols.at[:, 1].set(pos_lo.astype(jnp.bfloat16))
    kv_pack = jnp.concatenate((keys, values, pos_cols), axis=1)
    kv_all = lax.all_gather(kv_pack, CTX, axis=0, tiled=True)
    kv_width = keys.shape[1]
    k_piece = kv_all[:, :kv_width]
    v_piece = kv_all[:, kv_width : 2 * kv_width]
    pos_back = kv_all[:, 2 * kv_width :].astype(jnp.float32)
    k_pos = pos_back[:, 0] * 64.0 + pos_back[:, 1]
    q_pos = positions.astype(jnp.float32)
    count = k_piece.shape[0]
    k_three = k_piece.reshape(count, local_kv, HEAD)
    v_three = v_piece.reshape(count, local_kv, HEAD)
    scores = (
        jnp.einsum("tgjd,sgd->gjts", query_four, k_three, preferred_element_type=jnp.float32)
        * scale
    )
    visible = k_pos[None, :] <= q_pos[:, None]
    piece_top = jnp.max(jnp.where(visible, scores, jnp.float32(-1e30)), axis=-1)
    top_new = jnp.maximum(top_run, piece_top)
    weights = jnp.where(visible, jnp.exp(scores - top_new[..., None]), jnp.float32(0.0))
    total_new = jnp.sum(weights, axis=-1)
    mixed = jnp.einsum(
        "gjts,sgd->gjtd", weights.astype(jnp.bfloat16), v_three, preferred_element_type=jnp.float32
    )
    final_state = (top_new, total_new, mixed)
    top_run, total_run, accum = final_state
    normed = accum / total_run[..., None]
    attended = (
        jnp.transpose(normed, (2, 0, 1, 3))
        .reshape(tok_rows, local_heads * HEAD)
        .astype(jnp.bfloat16)
    )
    hidden_cols = w_gate.shape[1]
    both_weights = jnp.concatenate((w_gate, w_up), axis=1)
    pair_weights = lax.all_gather(both_weights, "cc", axis=1, tiled=True)
    x_half = lax.all_gather(x_normed, ("xh", "zz"), axis=0, tiled=True)
    block_terms = jnp.dot(
        x_half, pair_weights, preferred_element_type=jnp.float32
    ).astype(jnp.bfloat16)
    summed = lax.psum_scatter(
        block_terms, "mp", scatter_dimension=0, tiled=True
    ).astype(jnp.float32)
    width = 2 * hidden_cols
    per_core = []
    for owner in range(2):
        gate = summed[:, owner * width : owner * width + hidden_cols]
        up = summed[:, owner * width + hidden_cols : (owner + 1) * width]
        per_core.append((jax.nn.silu(gate) * up).astype(jnp.bfloat16))
    stacked = jnp.stack(per_core)
    core = lax.axis_index("cc")
    mine = stacked[core]
    other = stacked[1 - core]
    got = lax.ppermute(other, "cc", [(0, 1), (1, 0)])
    both = jnp.stack((mine, got))
    parity0 = both[core]
    parity1 = both[1 - core]
    rows = parity0.shape[0]
    chunk = tok_rows
    mlp_hidden = jnp.stack(
        (parity0.reshape(rows // chunk, chunk, hidden_cols), parity1.reshape(rows // chunk, chunk, hidden_cols)),
        axis=1,
    ).reshape(2 * rows, hidden_cols)
    return (attended, mlp_hidden)


def solution(mesh):
    n_ctx = mesh.shape["ctx"]
    n_mp = mesh.shape["mp"]
    fine = Mesh(mesh.devices.reshape(2, n_ctx // 4, 2, n_mp), ("xh", "zz", "cc", "mp"))
    return jax.shard_map(
        per_device,
        mesh=fine,
        in_specs=(
            P(CTX, "mp"),
            P(CTX, "mp"),
            P(CTX, "mp"),
            P(CTX),
            P(CTX, "mp"),
            P("mp", CTX),
            P("mp", CTX),
        ),
        out_specs=(P(CTX, "mp"), P("mp", CTX)),
        check_vma=False,
    )
```

```python
import jax
import jax.numpy as jnp
from jax import lax
from jax.sharding import PartitionSpec as P

HEAD = 128


def per_device(queries, keys, values, positions, x_normed, w_gate, w_up):
    tok_rows = queries.shape[0]
    local_heads = queries.shape[1] // HEAD
    local_kv = keys.shape[1] // HEAD
    group = local_heads // local_kv
    scale = HEAD ** (-0.5)
    query_four = queries.reshape(tok_rows, local_kv, group, HEAD)
    top_run = jnp.full((local_kv, group, tok_rows), -1e30, jnp.float32)
    pos_hi = positions // 64
    pos_lo = positions - pos_hi * 64
    pos_cols = jnp.zeros((tok_rows, HEAD), jnp.bfloat16)
    pos_cols = pos_cols.at[:, 0].set(pos_hi.astype(jnp.bfloat16))
    pos_cols = pos_cols.at[:, 1].set(pos_lo.astype(jnp.bfloat16))
    x_width = x_normed.shape[1]
    kv_width = keys.shape[1]
    pack = jnp.concatenate((x_normed, keys, values, pos_cols), axis=1)
    pack_all = lax.all_gather(pack, "ctx", axis=0, tiled=True)
    x_all = pack_all[:, :x_width]
    k_piece = pack_all[:, x_width : x_width + kv_width]
    v_piece = pack_all[:, x_width + kv_width : x_width + 2 * kv_width]
    pos_back = pack_all[:, x_width + 2 * kv_width :].astype(jnp.float32)
    k_pos = pos_back[:, 0] * 64.0 + pos_back[:, 1]
    q_pos = positions.astype(jnp.float32)
    count = k_piece.shape[0]
    k_three = k_piece.reshape(count, local_kv, HEAD)
    v_three = v_piece.reshape(count, local_kv, HEAD)
    scores = (
        jnp.einsum("tgjd,sgd->gjts", query_four, k_three, preferred_element_type=jnp.float32)
        * scale
    )
    visible = k_pos[None, :] <= q_pos[:, None]
    piece_top = jnp.max(jnp.where(visible, scores, jnp.float32(-1e30)), axis=-1)
    top_new = jnp.maximum(top_run, piece_top)
    weights = jnp.where(visible, jnp.exp(scores - top_new[..., None]), jnp.float32(0.0))
    total_new = jnp.sum(weights, axis=-1)
    mixed = jnp.einsum(
        "gjts,sgd->gjtd", weights.astype(jnp.bfloat16), v_three, preferred_element_type=jnp.float32
    )
    final_state = (top_new, total_new, mixed)
    top_run, total_run, accum = final_state
    normed = accum / total_run[..., None]
    attended = (
        jnp.transpose(normed, (2, 0, 1, 3))
        .reshape(tok_rows, local_heads * HEAD)
        .astype(jnp.bfloat16)
    )
    hidden_cols = w_gate.shape[1]
    both_weights = jnp.concatenate((w_gate, w_up), axis=1)
    block_terms = jnp.dot(
        x_all,
        both_weights,
        preferred_element_type=jnp.float32,
    ).astype(jnp.bfloat16)
    summed = lax.psum_scatter(
        block_terms.astype(jnp.float32).astype(jnp.bfloat16), "mp", scatter_dimension=0, tiled=True
    ).astype(jnp.float32)
    gate = summed[:, :hidden_cols]
    up = summed[:, hidden_cols:]
    mlp_hidden = (jax.nn.silu(gate) * up).astype(jnp.bfloat16)
    return (attended, mlp_hidden)


def solution(mesh):
    return jax.shard_map(
        per_device,
        mesh=mesh,
        in_specs=(
            P("ctx", "mp"),
            P("ctx", "mp"),
            P("ctx", "mp"),
            P("ctx"),
            P("ctx", "mp"),
            P("mp", "ctx"),
            P("mp", "ctx"),
        ),
        out_specs=(P("ctx", "mp"), P("mp", "ctx")),
        check_vma=False,
    )
```

```python
import jax
import jax.numpy as jnp
from jax import lax
from jax.sharding import PartitionSpec as P

HEAD = 128


def per_device(queries, keys, values, positions, x_normed, w_gate, w_up):
    tok_rows = queries.shape[0]
    local_heads = queries.shape[1] // HEAD
    local_kv = keys.shape[1] // HEAD
    group = local_heads // local_kv
    scale = HEAD ** (-0.5)
    query_four = queries.reshape(tok_rows, local_kv, group, HEAD)
    top_run = jnp.full((local_kv, group, tok_rows), -1e30, jnp.float32)
    pos_hi = positions // 64
    pos_lo = positions - pos_hi * 64
    col = lax.broadcasted_iota(jnp.int32, (tok_rows, HEAD), 1)
    pos_cols = jnp.where(
        col == 0, pos_hi[:, None], jnp.where(col == 1, pos_lo[:, None], 0)
    ).astype(jnp.bfloat16)
    x_width = x_normed.shape[1]
    kv_width = keys.shape[1]
    pack = jnp.concatenate((x_normed, keys, values, pos_cols), axis=1)
    pack_all = lax.all_gather(pack, "ctx", axis=0, tiled=True)
    x_all = pack_all[:, :x_width]
    k_piece = pack_all[:, x_width : x_width + kv_width]
    v_piece = pack_all[:, x_width + kv_width : x_width + 2 * kv_width]
    pos_back = pack_all[:, x_width + 2 * kv_width :].astype(jnp.float32)
    k_pos = pos_back[:, 0] * 64.0 + pos_back[:, 1]
    q_pos = positions.astype(jnp.float32)
    count = k_piece.shape[0]
    k_three = k_piece.reshape(count, local_kv, HEAD)
    v_three = v_piece.reshape(count, local_kv, HEAD)
    scores = (
        jnp.einsum("tgjd,sgd->gjts", query_four, k_three, preferred_element_type=jnp.float32)
        * scale
    )
    visible = k_pos[None, :] <= q_pos[:, None]
    piece_top = jnp.max(jnp.where(visible, scores, jnp.float32(-1e30)), axis=-1)
    top_new = jnp.maximum(top_run, piece_top)
    weights = jnp.where(visible, jnp.exp(scores - top_new[..., None]), jnp.float32(0.0))
    total_new = jnp.sum(weights, axis=-1)
    mixed = jnp.einsum(
        "gjts,sgd->gjtd", weights.astype(jnp.bfloat16), v_three, preferred_element_type=jnp.float32
    )
    final_state = (top_new, total_new, mixed)
    top_run, total_run, accum = final_state
    normed = accum / total_run[..., None]
    attended = (
        jnp.transpose(normed, (2, 0, 1, 3))
        .reshape(tok_rows, local_heads * HEAD)
        .astype(jnp.bfloat16)
    )
    hidden_cols = w_gate.shape[1]
    both_weights = jnp.concatenate((w_gate, w_up), axis=1)
    block_terms = jnp.dot(
        x_all,
        both_weights,
        preferred_element_type=jnp.float32,
    ).astype(jnp.bfloat16)
    summed = lax.psum_scatter(
        block_terms.astype(jnp.float32).astype(jnp.bfloat16), "mp", scatter_dimension=0, tiled=True
    ).astype(jnp.float32)
    gate = summed[:, :hidden_cols]
    up = summed[:, hidden_cols:]
    mlp_hidden = (jax.nn.silu(gate) * up).astype(jnp.bfloat16)
    return (attended, mlp_hidden)


def solution(mesh):
    return jax.shard_map(
        per_device,
        mesh=mesh,
        in_specs=(
            P("ctx", "mp"),
            P("ctx", "mp"),
            P("ctx", "mp"),
            P("ctx"),
            P("ctx", "mp"),
            P("mp", "ctx"),
            P("mp", "ctx"),
        ),
        out_specs=(P("ctx", "mp"), P("mp", "ctx")),
        check_vma=False,
    )
```

```python
import jax
import jax.numpy as jnp
from jax import lax
from jax.sharding import PartitionSpec as P

HEAD = 128


def per_device(queries, keys, values, positions, x_normed, w_gate, w_up):
    tok_rows = queries.shape[0]
    local_heads = queries.shape[1] // HEAD
    local_kv = keys.shape[1] // HEAD
    group = local_heads // local_kv
    scale = HEAD ** (-0.5)
    query_four = queries.reshape(tok_rows, local_kv, group, HEAD)
    top_run = jnp.full((local_kv, group, tok_rows), -1e30, jnp.float32)
    pos_hi = positions // 64
    pos_lo = positions - pos_hi * 64
    col = lax.broadcasted_iota(jnp.int32, (tok_rows, HEAD), 1)
    pos_cols = jnp.where(
        col == 0, pos_hi[:, None], jnp.where(col == 1, pos_lo[:, None], 0)
    ).astype(jnp.bfloat16)
    x_width = x_normed.shape[1]
    kv_width = keys.shape[1]
    pack = jnp.concatenate((x_normed, keys, values, pos_cols), axis=1)
    pack_all = lax.all_gather(pack, "ctx", axis=0, tiled=True)
    x_all = pack_all[:, :x_width]
    k_piece = pack_all[:, x_width : x_width + kv_width]
    v_piece = pack_all[:, x_width + kv_width : x_width + 2 * kv_width]
    pos_back = pack_all[:, x_width + 2 * kv_width :].astype(jnp.float32)
    k_pos = pos_back[:, 0] * 64.0 + pos_back[:, 1]
    q_pos = positions.astype(jnp.float32)
    count = k_piece.shape[0]
    k_three = k_piece.reshape(count, local_kv, HEAD)
    v_three = v_piece.reshape(count, local_kv, HEAD)
    scores = (
        jnp.einsum("tgjd,sgd->gjts", query_four, k_three, preferred_element_type=jnp.float32)
        * scale
    )
    visible = k_pos[None, :] <= q_pos[:, None]
    piece_top = jnp.max(jnp.where(visible, scores, jnp.float32(-1e30)), axis=-1)
    top_new = jnp.maximum(top_run, piece_top)
    weights = jnp.where(visible, jnp.exp(scores - top_new[..., None]), jnp.float32(0.0))
    total_new = jnp.sum(weights, axis=-1)
    mixed = jnp.einsum(
        "gjts,sgd->gjtd", weights.astype(jnp.bfloat16), v_three, preferred_element_type=jnp.float32
    )
    final_state = (top_new, total_new, mixed)
    top_run, total_run, accum = final_state
    normed = accum / total_run[..., None]
    attended = (
        jnp.transpose(normed, (2, 0, 1, 3))
        .reshape(tok_rows, local_heads * HEAD)
        .astype(jnp.bfloat16)
    )
    hidden_cols = w_gate.shape[1]
    both_weights = jnp.concatenate((w_gate, w_up), axis=1)
    block_terms = jnp.dot(
        x_all,
        both_weights,
        preferred_element_type=jnp.float32,
    ).astype(jnp.bfloat16)
    gate_sum = lax.psum_scatter(
        block_terms[:, :hidden_cols], "mp", scatter_dimension=0, tiled=True
    ).astype(jnp.float32)
    n_mp = lax.axis_size("mp")
    up_parts = lax.all_to_all(
        block_terms[:, hidden_cols:].reshape(n_mp, -1, hidden_cols), "mp", 0, 0, tiled=True
    )
    up_sum = up_parts.astype(jnp.float32).sum(axis=0)
    summed = jnp.concatenate((gate_sum, up_sum), axis=1)
    gate = summed[:, :hidden_cols]
    up = summed[:, hidden_cols:]
    mlp_hidden = (jax.nn.silu(gate) * up).astype(jnp.bfloat16)
    return (attended, mlp_hidden)


def solution(mesh):
    return jax.shard_map(
        per_device,
        mesh=mesh,
        in_specs=(
            P("ctx", "mp"),
            P("ctx", "mp"),
            P("ctx", "mp"),
            P("ctx"),
            P("ctx", "mp"),
            P("mp", "ctx"),
            P("mp", "ctx"),
        ),
        out_specs=(P("ctx", "mp"), P("mp", "ctx")),
        check_vma=False,
    )
```

```python
import jax
import jax.numpy as jnp
from jax import lax
from jax.sharding import PartitionSpec as P

HEAD = 128


def per_device(queries, keys, values, positions, x_normed, w_gate, w_up):
    tok_rows = queries.shape[0]
    local_heads = queries.shape[1] // HEAD
    local_kv = keys.shape[1] // HEAD
    group = local_heads // local_kv
    scale = HEAD ** (-0.5)
    query_four = queries.reshape(tok_rows, local_kv, group, HEAD)
    top_run = jnp.full((local_kv, group, tok_rows), -1e30, jnp.float32)
    pos_hi = positions // 64
    pos_lo = positions - pos_hi * 64
    col = lax.broadcasted_iota(jnp.int32, (tok_rows, HEAD), 1)
    pos_cols = jnp.where(
        col == 0, pos_hi[:, None], jnp.where(col == 1, pos_lo[:, None], 0)
    ).astype(jnp.bfloat16)
    x_width = x_normed.shape[1]
    kv_width = keys.shape[1]
    pack = jnp.concatenate((x_normed, keys, values, pos_cols), axis=1)
    pack_all = lax.all_gather(pack, "ctx", axis=0, tiled=True)
    x_all = pack_all[:, :x_width]
    k_piece = pack_all[:, x_width : x_width + kv_width]
    v_piece = pack_all[:, x_width + kv_width : x_width + 2 * kv_width]
    pos_back = pack_all[:, x_width + 2 * kv_width :].astype(jnp.float32)
    k_pos = pos_back[:, 0] * 64.0 + pos_back[:, 1]
    q_pos = positions.astype(jnp.float32)
    count = k_piece.shape[0]
    k_three = k_piece.reshape(count, local_kv, HEAD)
    v_three = v_piece.reshape(count, local_kv, HEAD)
    scores = (
        jnp.einsum("tgjd,sgd->gjts", query_four, k_three, preferred_element_type=jnp.float32)
        * scale
    )
    visible = k_pos[None, :] <= q_pos[:, None]
    piece_top = jnp.max(jnp.where(visible, scores, jnp.float32(-1e30)), axis=-1)
    top_new = jnp.maximum(top_run, piece_top)
    weights = jnp.where(visible, jnp.exp(scores - top_new[..., None]), jnp.float32(0.0))
    total_new = jnp.sum(weights, axis=-1)
    mixed = jnp.einsum(
        "gjts,sgd->gjtd", weights.astype(jnp.bfloat16), v_three, preferred_element_type=jnp.float32
    )
    final_state = (top_new, total_new, mixed)
    top_run, total_run, accum = final_state
    normed = accum / total_run[..., None]
    attended = (
        jnp.transpose(normed, (2, 0, 1, 3))
        .reshape(tok_rows, local_heads * HEAD)
        .astype(jnp.bfloat16)
    )
    hidden_cols = w_gate.shape[1]
    both_weights = jnp.concatenate((w_gate, w_up), axis=1)
    block_terms = jnp.dot(
        x_all,
        both_weights,
        preferred_element_type=jnp.float32,
    ).astype(jnp.bfloat16)
    n_mp = lax.axis_size("mp")
    parts = lax.all_to_all(
        block_terms.reshape(n_mp, -1, 2 * hidden_cols), "mp", 0, 0, tiled=True
    )
    summed = parts.astype(jnp.float32).sum(axis=0)
    gate = summed[:, :hidden_cols]
    up = summed[:, hidden_cols:]
    mlp_hidden = (jax.nn.silu(gate) * up).astype(jnp.bfloat16)
    return (attended, mlp_hidden)


def solution(mesh):
    return jax.shard_map(
        per_device,
        mesh=mesh,
        in_specs=(
            P("ctx", "mp"),
            P("ctx", "mp"),
            P("ctx", "mp"),
            P("ctx"),
            P("ctx", "mp"),
            P("mp", "ctx"),
            P("mp", "ctx"),
        ),
        out_specs=(P("ctx", "mp"), P("mp", "ctx")),
        check_vma=False,
    )
```

```python
import jax
import jax.numpy as jnp
from jax import lax
from jax.sharding import PartitionSpec as P

HEAD = 128


def per_device(queries, keys, values, positions, x_normed, w_gate, w_up):
    tok_rows = queries.shape[0]
    local_heads = queries.shape[1] // HEAD
    local_kv = keys.shape[1] // HEAD
    group = local_heads // local_kv
    scale = HEAD ** (-0.5)
    query_four = queries.reshape(tok_rows, local_kv, group, HEAD)
    top_run = jnp.full((local_kv, group, tok_rows), -1e30, jnp.float32)
    pos_hi = positions // 64
    pos_lo = positions - pos_hi * 64
    col = lax.broadcasted_iota(jnp.int32, (tok_rows, HEAD), 1)
    pos_cols = jnp.where(
        col == 0, pos_hi[:, None], jnp.where(col == 1, pos_lo[:, None], 0)
    ).astype(jnp.bfloat16)
    x_width = x_normed.shape[1]
    kv_width = keys.shape[1]
    pack = jnp.concatenate((x_normed, keys, values, pos_cols), axis=1)
    pack_all = lax.all_gather(pack, "ctx", axis=0, tiled=True)
    x_all = pack_all[:, :x_width]
    k_piece = pack_all[:, x_width : x_width + kv_width]
    v_piece = pack_all[:, x_width + kv_width : x_width + 2 * kv_width]
    pos_back = pack_all[:, x_width + 2 * kv_width :].astype(jnp.float32)
    k_pos = pos_back[:, 0] * 64.0 + pos_back[:, 1]
    q_pos = positions.astype(jnp.float32)
    count = k_piece.shape[0]
    k_three = k_piece.reshape(count, local_kv, HEAD)
    v_three = v_piece.reshape(count, local_kv, HEAD)
    scores = (
        jnp.einsum("tgjd,sgd->gjts", query_four, k_three, preferred_element_type=jnp.float32)
        * scale
    )
    visible = k_pos[None, :] <= q_pos[:, None]
    piece_top = jnp.max(jnp.where(visible, scores, jnp.float32(-1e30)), axis=-1)
    top_new = jnp.maximum(top_run, piece_top)
    weights = jnp.where(visible, jnp.exp(scores - top_new[..., None]), jnp.float32(0.0))
    total_new = jnp.sum(weights, axis=-1)
    mixed = jnp.einsum(
        "gjts,sgd->gjtd", weights.astype(jnp.bfloat16), v_three, preferred_element_type=jnp.float32
    )
    final_state = (top_new, total_new, mixed)
    top_run, total_run, accum = final_state
    normed = accum / total_run[..., None]
    attended = (
        jnp.transpose(normed, (2, 0, 1, 3))
        .reshape(tok_rows, local_heads * HEAD)
        .astype(jnp.bfloat16)
    )
    hidden_cols = w_gate.shape[1]
    both_weights = jnp.concatenate((w_gate, w_up), axis=1)
    block_terms = jnp.dot(
        x_all,
        both_weights,
        preferred_element_type=jnp.float32,
    ).astype(jnp.bfloat16)
    n_mp = lax.axis_size("mp")
    parts = lax.all_to_all(
        block_terms.reshape(n_mp, -1, 2 * hidden_cols), "mp", 0, 0, tiled=True
    )
    summed = parts[0].astype(jnp.float32)
    for index in range(1, n_mp):
        summed = summed + parts[index].astype(jnp.float32)
    gate = summed[:, :hidden_cols]
    up = summed[:, hidden_cols:]
    mlp_hidden = (jax.nn.silu(gate) * up).astype(jnp.bfloat16)
    return (attended, mlp_hidden)


def solution(mesh):
    return jax.shard_map(
        per_device,
        mesh=mesh,
        in_specs=(
            P("ctx", "mp"),
            P("ctx", "mp"),
            P("ctx", "mp"),
            P("ctx"),
            P("ctx", "mp"),
            P("mp", "ctx"),
            P("mp", "ctx"),
        ),
        out_specs=(P("ctx", "mp"), P("mp", "ctx")),
        check_vma=False,
    )
```
